768 devices in a mesh: dp: 96 (over z, y), tensor: 8 (over x, core).
Axes of the slice: x: 4, y: 8, z: 12, core: 2. Of those that a mesh axis runs over, the one named last changes fastest.
Arguments:
- tokens: bfloat16 [12288, 2048], P('dp', 'tensor'), may hold values from -6 to 6
- cotangent: bfloat16 [12288, 2048], P('dp', 'tensor'), may hold values from -6 to 6
- pair_ids: int32 [12288], P('dp'), may hold values from 0 to 99, as said below
- up_mask: int32 [100, 16, 64], P(None, None, 'tensor'), may hold values 0 or 1
- down_mask: int32 [100, 64, 16], P(None, 'tensor'), may hold values 0 or 1
- up_weight: bfloat16 [2048, 8192], P(None, 'tensor'), may hold values from -0.125 to 0.125
- down_weight: bfloat16 [96, 8192, 2048], P('dp', 'tensor'), may hold values from -0.0625 to 0.0625
Outputs:
- mixed: bfloat16 [12288, 2048], P('dp', 'tensor')
- token_grads: bfloat16 [12288, 2048], P('dp', 'tensor')
The draws below stay inside these ranges and needn't reach their ends.
Inputs may be any that keep to these rules, and one draw needn't show every extreme that they name: `pair_ids`: within each aligned block of 128 tokens (the tokens of one index of dp) at most 2 tokens belong to one language group; in every draw 8 groups hold exactly 2 tokens of every block.
All inputs are finite; a program needn't handle non-finite values. No bound on the sum of `up_mask` or of `down_mask` on one device may be relied on, other than what follows from the above.
Results may differ from the reference program's by a relative error of at most 0.014.
Values may be sent and summed in bfloat16 or wider, within the bound.
No kernel may reach another device: no remote copies, remote signals or barrier semaphores. Data moves between devices by JAX's collectives and lax.ppermute only.
A program may use at most 128 MiB of HBM per device.

```python
import jax
import jax.numpy as jnp
from jax import lax

D = 2048
FF = 8192
BLOCK = 128
PAIRS = 100
TOK_DEV = 128
OWNERS = 96
CAP = 2
HOT = 8
TOKENS = 12288
N_TENSOR = 8


def draw_pair_ids(key, part):
    slot_entries = OWNERS * CAP
    key_hot, key_score, key_choose, key_order = jax.random.split(key, 4)
    hottest = jax.random.permutation(key_hot, OWNERS)[:HOT]
    frequent_flag = jnp.any(jnp.arange(OWNERS)[:, None] == hottest[None, :], axis=1)
    slot_group_index = jnp.arange(slot_entries) // CAP
    extra_score = jnp.where(frequent_flag[slot_group_index], 1 << 29, 0).astype(jnp.int32)
    noise_portion = jax.random.randint(key_score, (OWNERS, slot_entries), 0, 1 << 18)
    ranking_values = noise_portion * slot_entries + jnp.arange(slot_entries, dtype=jnp.int32)[None, :] + extra_score[None, :]
    chosen = lax.top_k(ranking_values, TOK_DEV)[1]
    groups = chosen // CAP
    choices_here = (PAIRS - 1 - groups) // OWNERS + 1
    offsets = jax.random.randint(key_choose, groups.shape, 0, choices_here)
    pairs = groups + OWNERS * offsets
    order_keys = jax.random.split(key_order, OWNERS)
    pairs = jax.vmap(jax.random.permutation)(order_keys, pairs)
    return pairs.reshape(-1).astype(jnp.int32)


def touch_ends(values, key, smallest, largest):
    shape = values.shape
    index_at = [jax.random.randint(jax.random.fold_in(key, axis), (), 0, shape[axis]) for axis in range(len(shape))]
    values = values.at[tuple(index_at)].set(smallest)
    longest = shape.index(max(shape))
    index_at[longest] = (index_at[longest] + 1) % shape[longest]
    return values.at[tuple(index_at)].set(largest)


def block_scale(own_key, shape, shards, smallest, largest):
    loudness, own = 1.0, jax.random.fold_in(own_key, 6)
    for dim, parts in shards:
        draws = jnp.exp(jax.random.uniform(jax.random.fold_in(own, dim), (parts,), jnp.float32, smallest / len(shards), largest / len(shards)))
        loudness = loudness * jnp.repeat(draws, shape[dim] // parts).reshape([-1 if axis == dim else 1 for axis in range(len(shape))])
    return loudness


def bell_draw(rng, extent, scale, bound, pieces=(), kind=jnp.bfloat16):
    drawn = scale * jax.random.normal(rng, extent, jnp.float32)
    if pieces:
        drawn = drawn * block_scale(rng, extent, pieces, -0.22, 0.18)
    return jnp.clip(drawn, -bound, bound).astype(kind)


def setup_inputs(seed: int = 0) -> dict:
    seeds = jax.random.split(jax.random.key(seed), 8)
    tokens = bell_draw(seeds[0], (TOKENS, D), 1.0, 6.0, ((0, 96), (1, 8)))
    cotangent = bell_draw(seeds[1], (TOKENS, D), 1.0, 6.0, ((0, 96), (1, 8)))
    pair_ids = draw_pair_ids(jax.random.fold_in(seeds[7], 71), 0)
    up_mask = touch_ends((jax.random.randint(seeds[3], (PAIRS, D // BLOCK, FF // BLOCK), 0, 4) < 3).astype(jnp.int32), jax.random.fold_in(seeds[3], 1), 0, 1)
    down_mask = touch_ends((jax.random.randint(seeds[4], (PAIRS, FF // BLOCK, D // BLOCK), 0, 4) < 3).astype(jnp.int32), jax.random.fold_in(seeds[4], 1), 0, 1)
    up_weight = bell_draw(seeds[5], (D, FF), D ** -0.5, 0.125, ((1, 8),))
    down_weight = bell_draw(seeds[6], (OWNERS, FF, D), FF ** -0.5, 0.0625, ((0, 96), (1, 8)))
    return {"tokens": tokens, "cotangent": cotangent, "pair_ids": pair_ids, "up_mask": up_mask, "down_mask": down_mask, "up_weight": up_weight, "down_weight": down_weight}


highest = lax.Precision.HIGHEST

def product_plain(inputs, weight, masks):
    columns = weight.shape[1]
    blocks_out = columns // BLOCK
    spread = jnp.repeat(jnp.transpose(masks, (2, 0, 1)), BLOCK, axis=2)
    masked = inputs.astype(jnp.float32)[None, :, :] * spread
    weight_tiles = weight.astype(jnp.float32).reshape(weight.shape[0], blocks_out, BLOCK)
    result = jnp.einsum('nrk,knc->rnc', masked, weight_tiles, precision=highest)
    return result.reshape(inputs.shape[0], columns)

def product_turned(inputs, weight, masks):
    columns = weight.shape[0]
    blocks_out = columns // BLOCK
    spread = jnp.repeat(jnp.transpose(masks, (1, 0, 2)), BLOCK, axis=2)
    masked = inputs.astype(jnp.float32)[None, :, :] * spread
    weight_tiles = weight.astype(jnp.float32).reshape(blocks_out, BLOCK, weight.shape[1])
    result = jnp.einsum('nrk,nck->rnc', masked, weight_tiles, precision=highest)
    return result.reshape(inputs.shape[0], columns)

def mask_rows(mask_table, pairs_here):
    safe_pairs = jnp.maximum(pairs_here, 0)
    looked = mask_table[safe_pairs].astype(jnp.float32)
    return jnp.where((pairs_here >= 0)[:, None, None], looked, jnp.zeros_like(looked))

def slot_table(pair_ids):
    target = (pair_ids % OWNERS).reshape(OWNERS, TOK_DEV)
    matches = (target[:, :, None] == jnp.arange(OWNERS, dtype=jnp.int32)[None, None, :]).astype(jnp.int32)
    before = lax.optimization_barrier(jnp.sum((jnp.cumsum(matches, axis=1) - matches) * matches, axis=2))
    source = jnp.arange(OWNERS, dtype=jnp.int32)[:, None]
    position = ((target * OWNERS + source) * CAP + before).astype(jnp.int32)
    token_index = jnp.arange(TOKENS, dtype=jnp.int32)
    filled = jnp.full((OWNERS * OWNERS * CAP,), TOKENS, jnp.int32).at[position.reshape(-1)].set(token_index)
    return filled.reshape(OWNERS, OWNERS * CAP)

def shard_sums_down(hidden, down_group, down_rows):
    width = FF // N_TENSOR
    blocks = width // BLOCK
    total = jnp.zeros((hidden.shape[0], D), jnp.float32)
    for shard in range(N_TENSOR):
        part = product_plain(hidden[:, shard * width:(shard + 1) * width], down_group[shard * width:(shard + 1) * width, :], down_rows[:, shard * blocks:(shard + 1) * blocks, :])
        rounded = lax.optimization_barrier(part.astype(jnp.bfloat16))
        total = total + rounded.astype(jnp.float32)
    return total.astype(jnp.bfloat16)

def shard_sums_up(grad_pre, up_weight, up_rows):
    width = FF // N_TENSOR
    blocks = width // BLOCK
    total = jnp.zeros((grad_pre.shape[0], D), jnp.float32)
    for shard in range(N_TENSOR):
        part = product_turned(grad_pre[:, shard * width:(shard + 1) * width], up_weight[:, shard * width:(shard + 1) * width], up_rows[:, :, shard * blocks:(shard + 1) * blocks])
        rounded = lax.optimization_barrier(part.astype(jnp.bfloat16))
        total = total + rounded.astype(jnp.float32)
    return total.astype(jnp.bfloat16)

def reference(tokens, cotangent, pair_ids, up_mask, down_mask, up_weight, down_weight):
    pair_table = slot_table(pair_ids)
    padded_tokens = jnp.concatenate([tokens, jnp.zeros((1, D), tokens.dtype)], axis=0)
    padded_grads = jnp.concatenate([cotangent, jnp.zeros((1, D), cotangent.dtype)], axis=0)
    padded_pairs = jnp.concatenate([pair_ids, jnp.full((1,), -1, jnp.int32)]).astype(jnp.int32)

    def one_group(packed):
        indices, down_group = packed
        pairs_here = padded_pairs[indices]
        up_rows = mask_rows(up_mask, pairs_here)
        down_rows = mask_rows(down_mask, pairs_here)
        before_act = product_plain(padded_tokens[indices], up_weight, up_rows)
        activated, backward_function = jax.vjp(jax.nn.gelu, before_act)
        hidden = activated.astype(jnp.bfloat16)
        mixed_rows = shard_sums_down(hidden, down_group, down_rows)
        grad_hidden = product_turned(padded_grads[indices], down_group, down_rows)
        grad_pre = backward_function(grad_hidden)[0].astype(jnp.bfloat16)
        input_rows = shard_sums_up(grad_pre, up_weight, up_rows)
        return (mixed_rows, input_rows)
    mixed_all, grads_all = lax.map(one_group, (pair_table, down_weight))
    flat_index = pair_table.reshape(-1)
    mixed = jnp.zeros((TOKENS + 1, D), jnp.bfloat16).at[flat_index].set(mixed_all.reshape(-1, D))[:TOKENS]
    token_grads = jnp.zeros((TOKENS + 1, D), jnp.bfloat16).at[flat_index].set(grads_all.reshape(-1, D))[:TOKENS]
    return (mixed, token_grads)
```

```python
import functools

import jax
import jax.numpy as jnp
from jax import lax
from jax.experimental import pallas as pl
from jax.sharding import PartitionSpec as P

BLOCK = 128
STEPS = 4


def picked_masks(mask_table, pairs_here, order):
    table = jnp.transpose(mask_table, order)
    pair_count, blocks_out, blocks_in = table.shape
    table = jnp.pad(table, ((0, 0), (0, 0), (0, BLOCK - blocks_in)))
    picker = (pairs_here[:, None] == jnp.arange(pair_count, dtype=jnp.int32)[None, :]).astype(
        jnp.bfloat16
    )
    flattened = table.reshape(pair_count, -1).astype(jnp.bfloat16)
    looked = jnp.dot(picker, flattened, preferred_element_type=jnp.float32).astype(jnp.bfloat16)
    looked = looked.reshape(pairs_here.shape[0], blocks_out, BLOCK)
    return jnp.transpose(looked, (1, 0, 2)), blocks_in


def masked_kernel(x_ref, m_ref, e_ref, w_ref, o_ref, *, per, turned):
    x = x_ref[...]
    for b in range(per):
        spread = jnp.dot(m_ref[b], e_ref[...], preferred_element_type=jnp.float32)
        masked = x * spread.astype(x.dtype)
        if turned:
            w = w_ref[b * BLOCK:(b + 1) * BLOCK, :]
            acc = lax.dot_general(
                masked, w, (((1,), (1,)), ((), ())), preferred_element_type=jnp.float32
            )
        else:
            w = w_ref[:, b * BLOCK:(b + 1) * BLOCK]
            acc = jnp.dot(masked, w, preferred_element_type=jnp.float32)
        o_ref[:, b * BLOCK:(b + 1) * BLOCK] = acc.astype(o_ref.dtype)


def masked_product(x, masks, blocks_in, weight, turned, out_dtype):
    rows, width = x.shape
    blocks_out = masks.shape[0]
    per = max(1, blocks_out // STEPS)
    steps = blocks_out // per
    cols = per * BLOCK
    blk = width // blocks_in
    expand = (
        jnp.arange(width, dtype=jnp.int32)[None, :] // blk == jnp.arange(BLOCK, dtype=jnp.int32)[:, None]
    ).astype(x.dtype)
    if turned:
        w_spec = pl.BlockSpec((cols, width), lambda j: (j, 0))
    else:
        w_spec = pl.BlockSpec((width, cols), lambda j: (0, j))
    return pl.pallas_call(
        functools.partial(masked_kernel, per=per, turned=turned),
        grid=(steps,),
        in_specs=[
            pl.BlockSpec((rows, width), lambda j: (0, 0)),
            pl.BlockSpec((per, rows, BLOCK), lambda j: (j, 0, 0)),
            pl.BlockSpec((BLOCK, width), lambda j: (0, 0)),
            w_spec,
        ],
        out_specs=pl.BlockSpec((rows, cols), lambda j: (0, j)),
        out_shape=jax.ShapeDtypeStruct((rows, blocks_out * BLOCK), out_dtype),
    )(x, masks, expand, weight)


def per_device(tokens, cotangent, pair_ids, up_mask, down_mask, up_weight, down_weight):
    groups = lax.axis_size("dp")
    tok_count, piece = tokens.shape
    capacity = max(2, (3 * tok_count + 2 * groups - 1) // (2 * groups))
    slot_count = groups * capacity
    target = pair_ids % groups
    matches = (target[:, None] == jnp.arange(groups, dtype=jnp.int32)[None, :]).astype(jnp.int32)
    before = jnp.sum((jnp.cumsum(matches, axis=0) - matches) * matches, axis=1)
    position = target * capacity + before
    placing = position[None, :] == jnp.arange(slot_count, dtype=jnp.int32)[:, None]
    placer = placing.astype(jnp.bfloat16)
    slot_pairs = jnp.sum(jnp.where(placing, pair_ids[None, :] + 1, 0), axis=1) - 1

    payload = jnp.concatenate([tokens, cotangent], axis=1)
    outgoing = jnp.dot(placer, payload, preferred_element_type=jnp.float32).astype(jnp.bfloat16)
    pair_cols = jnp.broadcast_to(slot_pairs.astype(jnp.bfloat16)[:, None], (slot_count, BLOCK))
    outgoing = jnp.concatenate([outgoing, pair_cols], axis=1)
    arrived = lax.all_to_all(
        outgoing.reshape(groups, capacity, -1), "dp", split_axis=0, concat_axis=0, tiled=True
    ).reshape(slot_count, -1)
    pairs_here = arrived[:, 2 * piece].astype(jnp.int32)

    both = jnp.stack([arrived[:, :piece], arrived[:, piece:2 * piece]])
    gathered = lax.all_gather(both, "tensor", axis=2, tiled=True)
    rows_in, grad_rows = gathered[0], gathered[1]

    up_fwd, up_in = picked_masks(up_mask, pairs_here, (0, 2, 1))
    up_bwd, up_out = picked_masks(up_mask, pairs_here, (0, 1, 2))
    down_fwd, down_in = picked_masks(down_mask, pairs_here, (0, 2, 1))
    down_bwd, down_out = picked_masks(down_mask, pairs_here, (0, 1, 2))
    down_local = down_weight[0]

    before_act = masked_product(rows_in, up_fwd, up_in, up_weight, False, jnp.float32)
    activated, backward_function = jax.vjp(jax.nn.gelu, before_act)
    hidden = activated.astype(jnp.bfloat16)
    mixed_part = masked_product(hidden, down_fwd, down_in, down_local, False, jnp.bfloat16)
    grad_hidden = masked_product(grad_rows, down_bwd, down_out, down_local, True, jnp.float32)
    grad_pre = backward_function(grad_hidden)[0].astype(jnp.bfloat16)
    input_part = masked_product(grad_pre, up_bwd, up_out, up_weight, True, jnp.bfloat16)

    parts = jnp.stack([mixed_part, input_part])
    summed = lax.psum_scatter(parts, "tensor", scatter_dimension=2, tiled=True)
    summed = summed.astype(jnp.float32).astype(jnp.bfloat16)

    back = jnp.transpose(summed, (1, 0, 2)).reshape(groups, capacity, 2 * piece)
    returned = lax.all_to_all(back, "dp", split_axis=0, concat_axis=0, tiled=True)
    flattened = returned.reshape(slot_count, 2 * piece)
    results = jnp.dot(placer.T, flattened, preferred_element_type=jnp.float32).astype(jnp.bfloat16)
    return (results[:, :piece], results[:, piece:])


def solution(mesh):
    return jax.shard_map(
        per_device,
        mesh=mesh,
        in_specs=(
            P("dp", "tensor"),
            P("dp", "tensor"),
            P("dp"),
            P(None, None, "tensor"),
            P(None, "tensor", None),
            P(None, "tensor"),
            P("dp", "tensor", None),
        ),
        out_specs=(P("dp", "tensor"), P("dp", "tensor")),
        check_vma=False,
    )
```

```python
import functools

import jax
import jax.numpy as jnp
from jax import lax
from jax.experimental import pallas as pl
from jax.sharding import PartitionSpec as P

BLOCK = 128
STEPS = 4


def picked_masks(mask_table, pairs_here, order):
    table = jnp.transpose(mask_table, order)
    pair_count, blocks_out, blocks_in = table.shape
    table = jnp.pad(table, ((0, 0), (0, 0), (0, BLOCK - blocks_in)))
    picker = (pairs_here[:, None] == jnp.arange(pair_count, dtype=jnp.int32)[None, :]).astype(
        jnp.bfloat16
    )
    flattened = table.reshape(pair_count, -1).astype(jnp.bfloat16)
    looked = jnp.dot(picker, flattened, preferred_element_type=jnp.float32).astype(jnp.bfloat16)
    looked = looked.reshape(pairs_here.shape[0], blocks_out, BLOCK)
    return jnp.transpose(looked, (1, 0, 2)), blocks_in


def masked_kernel(x_ref, m_ref, e_ref, w_ref, o_ref, *, per, turned):
    x = x_ref[...]
    for b in range(per):
        spread = jnp.dot(m_ref[b], e_ref[...], preferred_element_type=jnp.float32).astype(x.dtype)
        masked = x * spread
        if turned:
            w = w_ref[b * BLOCK:(b + 1) * BLOCK, :]
            acc = lax.dot_general(
                masked, w, (((1,), (1,)), ((), ())), preferred_element_type=jnp.float32
            )
        else:
            w = w_ref[:, b * BLOCK:(b + 1) * BLOCK]
            acc = jnp.dot(masked, w, preferred_element_type=jnp.float32)
        o_ref[:, b * BLOCK:(b + 1) * BLOCK] = acc.astype(o_ref.dtype)


def masked_product(x, masks, blocks_in, weight, turned, out_dtype):
    rows, width = x.shape
    blocks_out = masks.shape[0]
    per = max(1, blocks_out // STEPS)
    steps = blocks_out // per
    cols = per * BLOCK
    blk = width // blocks_in
    expand = (
        jnp.arange(width, dtype=jnp.int32)[None, :] // blk == jnp.arange(BLOCK, dtype=jnp.int32)[:, None]
    ).astype(x.dtype)
    if turned:
        w_spec = pl.BlockSpec((cols, width), lambda j: (j, 0))
    else:
        w_spec = pl.BlockSpec((width, cols), lambda j: (0, j))
    return pl.pallas_call(
        functools.partial(masked_kernel, per=per, turned=turned),
        grid=(steps,),
        in_specs=[
            pl.BlockSpec((rows, width), lambda j: (0, 0)),
            pl.BlockSpec((per, rows, BLOCK), lambda j: (j, 0, 0)),
            pl.BlockSpec((BLOCK, width), lambda j: (0, 0)),
            w_spec,
        ],
        out_specs=pl.BlockSpec((rows, cols), lambda j: (0, j)),
        out_shape=jax.ShapeDtypeStruct((rows, blocks_out * BLOCK), out_dtype),
    )(x, masks, expand, weight)


def per_device(tokens, cotangent, pair_ids, up_mask, down_mask, up_weight, down_weight):
    groups = lax.axis_size("dp")
    tok_count, piece = tokens.shape
    capacity = max(2, (3 * tok_count + 2 * groups - 1) // (2 * groups))
    slot_count = groups * capacity
    target = pair_ids % groups
    matches = (target[:, None] == jnp.arange(groups, dtype=jnp.int32)[None, :]).astype(jnp.int32)
    before = jnp.sum((jnp.cumsum(matches, axis=0) - matches) * matches, axis=1)
    position = target * capacity + before
    placing = position[None, :] == jnp.arange(slot_count, dtype=jnp.int32)[:, None]
    placer = placing.astype(jnp.bfloat16)
    slot_pairs = jnp.sum(jnp.where(placing, pair_ids[None, :] + 1, 0), axis=1) - 1

    payload = jnp.concatenate([tokens, cotangent], axis=1)
    outgoing = jnp.dot(placer, payload, preferred_element_type=jnp.float32).astype(jnp.bfloat16)
    feat_rows = outgoing.reshape(groups, capacity * 2 * piece // BLOCK, BLOCK)
    pair_rows = jnp.broadcast_to(
        slot_pairs.astype(jnp.bfloat16).reshape(groups, capacity, 1), (groups, capacity, BLOCK)
    )
    used = feat_rows.shape[1] + capacity
    tile_rows = -(-used // 16) * 16
    filler = jnp.zeros((groups, tile_rows - used, BLOCK), jnp.bfloat16)
    outgoing = jnp.concatenate([feat_rows, pair_rows, filler], axis=1)
    arrived = lax.all_to_all(outgoing, "dp", split_axis=0, concat_axis=0, tiled=True)
    feats = arrived[:, :feat_rows.shape[1], :].reshape(slot_count, 2 * piece)
    pairs_here = arrived[:, feat_rows.shape[1]:used, 0].reshape(slot_count).astype(jnp.int32)

    both = jnp.stack([feats[:, :piece], feats[:, piece:]])
    gathered = lax.all_gather(both, "tensor", axis=0, tiled=False)
    shards = gathered.shape[0]
    gathered = jnp.transpose(gathered, (1, 2, 0, 3)).reshape(2, slot_count, shards * piece)
    rows_in, grad_rows = gathered[0], gathered[1]

    up_fwd, up_in = picked_masks(up_mask, pairs_here, (0, 2, 1))
    up_bwd, up_out = picked_masks(up_mask, pairs_here, (0, 1, 2))
    down_fwd, down_in = picked_masks(down_mask, pairs_here, (0, 2, 1))
    down_bwd, down_out = picked_masks(down_mask, pairs_here, (0, 1, 2))
    down_local = down_weight[0]

    before_act = masked_product(rows_in, up_fwd, up_in, up_weight, False, jnp.float32)
    activated, backward_function = jax.vjp(jax.nn.gelu, before_act)
    hidden = activated.astype(jnp.bfloat16)
    mixed_part = masked_product(hidden, down_fwd, down_in, down_local, False, jnp.bfloat16)
    grad_hidden = masked_product(grad_rows, down_bwd, down_out, down_local, True, jnp.float32)
    grad_pre = backward_function(grad_hidden)[0].astype(jnp.bfloat16)
    input_part = masked_product(grad_pre, up_bwd, up_out, up_weight, True, jnp.bfloat16)

    parts = jnp.stack([mixed_part, input_part]).reshape(2, slot_count, shards, piece)
    parts = jnp.transpose(parts, (2, 0, 1, 3))
    summed = lax.psum_scatter(parts, "tensor", scatter_dimension=0, tiled=False)
    summed = summed.astype(jnp.float32).astype(jnp.bfloat16)

    back = jnp.transpose(summed, (1, 0, 2)).reshape(groups, capacity * 2 * piece // BLOCK, BLOCK)
    returned = lax.all_to_all(back, "dp", split_axis=0, concat_axis=0, tiled=True)
    flattened = returned.reshape(slot_count, 2 * piece)
    results = jnp.dot(placer.T, flattened, preferred_element_type=jnp.float32).astype(jnp.bfloat16)
    return (results[:, :piece], results[:, piece:])


def solution(mesh):
    return jax.shard_map(
        per_device,
        mesh=mesh,
        in_specs=(
            P("dp", "tensor"),
            P("dp", "tensor"),
            P("dp"),
            P(None, None, "tensor"),
            P(None, "tensor", None),
            P(None, "tensor"),
            P("dp", "tensor", None),
        ),
        out_specs=(P("dp", "tensor"), P("dp", "tensor")),
        check_vma=False,
    )
```

```python
import functools

import jax
import jax.numpy as jnp
from jax import lax
from jax.experimental import pallas as pl
from jax.sharding import PartitionSpec as P

BLOCK = 128
STEPS = 4


def picked_masks(mask_table, pairs_here, order):
    table = jnp.transpose(mask_table, order)
    pair_count, blocks_out, blocks_in = table.shape
    table = jnp.pad(table, ((0, 0), (0, 0), (0, BLOCK - blocks_in)))
    picker = (pairs_here[:, None] == jnp.arange(pair_count, dtype=jnp.int32)[None, :]).astype(
        jnp.bfloat16
    )
    flattened = table.reshape(pair_count, -1).astype(jnp.bfloat16)
    looked = jnp.dot(picker, flattened, preferred_element_type=jnp.float32).astype(jnp.bfloat16)
    looked = looked.reshape(pairs_here.shape[0], blocks_out, BLOCK)
    return jnp.transpose(looked, (1, 0, 2)), blocks_in


def masked_kernel(x_ref, m_ref, e_ref, w_ref, o_ref, *, per, turned, piece):
    x = x_ref[...]
    for b in range(per):
        spread = jnp.dot(m_ref[b], e_ref[...], preferred_element_type=jnp.float32).astype(x.dtype)
        masked = x * spread
        if turned:
            w = w_ref[b * BLOCK:(b + 1) * BLOCK, :]
            acc = lax.dot_general(
                masked, w, (((1,), (1,)), ((), ())), preferred_element_type=jnp.float32
            )
        else:
            w = w_ref[:, b * BLOCK:(b + 1) * BLOCK]
            acc = jnp.dot(masked, w, preferred_element_type=jnp.float32)
        if piece:
            at = b * BLOCK
            o_ref[at // piece, :, at % piece:at % piece + BLOCK] = acc.astype(o_ref.dtype)
        else:
            o_ref[:, b * BLOCK:(b + 1) * BLOCK] = acc.astype(o_ref.dtype)


def masked_product(x, masks, blocks_in, weight, turned, out_dtype, piece=0):
    rows, width = x.shape
    blocks_out = masks.shape[0]
    per = max(1, blocks_out // STEPS)
    steps = blocks_out // per
    cols = per * BLOCK
    blk = width // blocks_in
    expand = (
        jnp.arange(width, dtype=jnp.int32)[None, :] // blk == jnp.arange(BLOCK, dtype=jnp.int32)[:, None]
    ).astype(x.dtype)
    if turned:
        w_spec = pl.BlockSpec((cols, width), lambda j: (j, 0))
    else:
        w_spec = pl.BlockSpec((width, cols), lambda j: (0, j))
    if piece:
        out_spec = pl.BlockSpec((cols // piece, rows, piece), lambda j: (j, 0, 0))
        out_shape = (blocks_out * BLOCK // piece, rows, piece)
    else:
        out_spec = pl.BlockSpec((rows, cols), lambda j: (0, j))
        out_shape = (rows, blocks_out * BLOCK)
    return pl.pallas_call(
        functools.partial(masked_kernel, per=per, turned=turned, piece=piece),
        grid=(steps,),
        in_specs=[
            pl.BlockSpec((rows, width), lambda j: (0, 0)),
            pl.BlockSpec((per, rows, BLOCK), lambda j: (j, 0, 0)),
            pl.BlockSpec((BLOCK, width), lambda j: (0, 0)),
            w_spec,
        ],
        out_specs=out_spec,
        out_shape=jax.ShapeDtypeStruct(out_shape, out_dtype),
    )(x, masks, expand, weight)


def settle(part):
    arrived = lax.all_to_all(part, "tensor", split_axis=0, concat_axis=0, tiled=True)
    return jnp.sum(arrived.astype(jnp.float32), axis=0).astype(jnp.bfloat16)


def per_device(tokens, cotangent, pair_ids, up_mask, down_mask, up_weight, down_weight):
    groups = lax.axis_size("dp")
    tok_count, piece = tokens.shape
    capacity = max(2, (3 * tok_count + 2 * groups - 1) // (2 * groups))
    slot_count = groups * capacity
    target = pair_ids % groups
    matches = (target[:, None] == jnp.arange(groups, dtype=jnp.int32)[None, :]).astype(jnp.int32)
    before = jnp.sum((jnp.cumsum(matches, axis=0) - matches) * matches, axis=1)
    position = target * capacity + before
    placing = position[None, :] == jnp.arange(slot_count, dtype=jnp.int32)[:, None]
    placer = placing.astype(jnp.bfloat16)
    slot_pairs = jnp.sum(jnp.where(placing, pair_ids[None, :] + 1, 0), axis=1) - 1

    payload = jnp.concatenate([tokens, cotangent], axis=1)
    outgoing = jnp.dot(placer, payload, preferred_element_type=jnp.float32).astype(jnp.bfloat16)
    feat_rows = outgoing.reshape(groups, capacity * 2 * piece // BLOCK, BLOCK)
    pair_rows = jnp.broadcast_to(
        slot_pairs.astype(jnp.bfloat16).reshape(groups, capacity, 1), (groups, capacity, BLOCK)
    )
    used = feat_rows.shape[1] + capacity
    tile_rows = -(-used // 16) * 16
    filler = jnp.zeros((groups, tile_rows - used, BLOCK), jnp.bfloat16)
    outgoing = jnp.concatenate([feat_rows, pair_rows, filler], axis=1)
    arrived = lax.all_to_all(outgoing, "dp", split_axis=0, concat_axis=0, tiled=True)
    feats = arrived[:, :feat_rows.shape[1], :].reshape(slot_count, 2 * piece)
    pairs_here = arrived[:, feat_rows.shape[1]:used, 0].reshape(slot_count).astype(jnp.int32)

    both = jnp.stack([feats[:, :piece], feats[:, piece:]])
    gathered = lax.all_gather(both, "tensor", axis=0, tiled=False)
    shards = gathered.shape[0]
    gathered = jnp.transpose(gathered, (1, 2, 0, 3)).reshape(2, slot_count, shards * piece)
    rows_in, grad_rows = gathered[0], gathered[1]

    up_fwd, up_in = picked_masks(up_mask, pairs_here, (0, 2, 1))
    up_bwd, up_out = picked_masks(up_mask, pairs_here, (0, 1, 2))
    down_fwd, down_in = picked_masks(down_mask, pairs_here, (0, 2, 1))
    down_bwd, down_out = picked_masks(down_mask, pairs_here, (0, 1, 2))
    down_local = down_weight[0]

    before_act = masked_product(rows_in, up_fwd, up_in, up_weight, False, jnp.float32)
    activated, backward_function = jax.vjp(jax.nn.gelu, before_act)
    hidden = activated.astype(jnp.bfloat16)
    mixed_part = masked_product(hidden, down_fwd, down_in, down_local, False, jnp.bfloat16, piece)
    mixed_sum = settle(mixed_part)
    grad_hidden = masked_product(grad_rows, down_bwd, down_out, down_local, True, jnp.float32)
    grad_pre = backward_function(grad_hidden)[0].astype(jnp.bfloat16)
    input_part = masked_product(grad_pre, up_bwd, up_out, up_weight, True, jnp.bfloat16, piece)
    input_sum = settle(input_part)

    summed = jnp.stack([mixed_sum, input_sum])

    back = jnp.transpose(summed, (1, 0, 2)).reshape(groups, capacity * 2 * piece // BLOCK, BLOCK)
    returned = lax.all_to_all(back, "dp", split_axis=0, concat_axis=0, tiled=True)
    flattened = returned.reshape(slot_count, 2 * piece)
    results = jnp.dot(placer.T, flattened, preferred_element_type=jnp.float32).astype(jnp.bfloat16)
    return (results[:, :piece], results[:, piece:])


def solution(mesh):
    return jax.shard_map(
        per_device,
        mesh=mesh,
        in_specs=(
            P("dp", "tensor"),
            P("dp", "tensor"),
            P("dp"),
            P(None, None, "tensor"),
            P(None, "tensor", None),
            P(None, "tensor"),
            P("dp", "tensor", None),
        ),
        out_specs=(P("dp", "tensor"), P("dp", "tensor")),
        check_vma=False,
    )
```

```python
import functools

import jax
import jax.numpy as jnp
from jax import lax
from jax.experimental import pallas as pl
from jax.sharding import PartitionSpec as P

BLOCK = 128
STEPS = 4


def picked_masks(mask_table, pairs_here, order):
    table = jnp.transpose(mask_table, order)
    pair_count, blocks_out, blocks_in = table.shape
    table = jnp.pad(table, ((0, 0), (0, 0), (0, BLOCK - blocks_in)))
    picker = (pairs_here[:, None] == jnp.arange(pair_count, dtype=jnp.int32)[None, :]).astype(
        jnp.bfloat16
    )
    flattened = table.reshape(pair_count, -1).astype(jnp.bfloat16)
    looked = jnp.dot(picker, flattened, preferred_element_type=jnp.float32).astype(jnp.bfloat16)
    looked = looked.reshape(pairs_here.shape[0], blocks_out, BLOCK)
    return jnp.transpose(looked, (1, 0, 2)), blocks_in


def masked_kernel(x_ref, m_ref, e_ref, w_ref, o_ref, *, per, turned, piece):
    x = x_ref[...]
    for b in range(per):
        spread = jnp.dot(m_ref[b], e_ref[...], preferred_element_type=jnp.float32).astype(x.dtype)
        masked = x * spread
        if turned:
            w = w_ref[b * BLOCK:(b + 1) * BLOCK, :]
            acc = lax.dot_general(
                masked, w, (((1,), (1,)), ((), ())), preferred_element_type=jnp.float32
            )
        else:
            w = w_ref[:, b * BLOCK:(b + 1) * BLOCK]
            acc = jnp.dot(masked, w, preferred_element_type=jnp.float32)
        if piece:
            at = b * BLOCK
            o_ref[at // piece, :, at % piece:at % piece + BLOCK] = acc.astype(o_ref.dtype)
        else:
            o_ref[:, b * BLOCK:(b + 1) * BLOCK] = acc.astype(o_ref.dtype)


def masked_product(x, masks, blocks_in, weight, turned, out_dtype, piece=0):
    rows, width = x.shape
    blocks_out = masks.shape[0]
    per = max(1, blocks_out // STEPS)
    steps = blocks_out // per
    cols = per * BLOCK
    blk = width // blocks_in
    expand = (
        jnp.arange(width, dtype=jnp.int32)[None, :] // blk == jnp.arange(BLOCK, dtype=jnp.int32)[:, None]
    ).astype(x.dtype)
    if turned:
        w_spec = pl.BlockSpec((cols, width), lambda j: (j, 0))
    else:
        w_spec = pl.BlockSpec((width, cols), lambda j: (0, j))
    if piece:
        out_spec = pl.BlockSpec((cols // piece, rows, piece), lambda j: (j, 0, 0))
        out_shape = (blocks_out * BLOCK // piece, rows, piece)
    else:
        out_spec = pl.BlockSpec((rows, cols), lambda j: (0, j))
        out_shape = (rows, blocks_out * BLOCK)
    return pl.pallas_call(
        functools.partial(masked_kernel, per=per, turned=turned, piece=piece),
        grid=(steps,),
        in_specs=[
            pl.BlockSpec((rows, width), lambda j: (0, 0)),
            pl.BlockSpec((per, rows, BLOCK), lambda j: (j, 0, 0)),
            pl.BlockSpec((BLOCK, width), lambda j: (0, 0)),
            w_spec,
        ],
        out_specs=out_spec,
        out_shape=jax.ShapeDtypeStruct(out_shape, out_dtype),
    )(x, masks, expand, weight)


def settle(part):
    arrived = lax.all_to_all(part, "tensor", split_axis=0, concat_axis=0, tiled=True)
    return jnp.sum(arrived.astype(jnp.float32), axis=0).astype(jnp.bfloat16)


def per_device(tokens, cotangent, pair_ids, up_mask, down_mask, up_weight, down_weight):
    groups = lax.axis_size("dp")
    tok_count, piece = tokens.shape
    capacity = max(2, (3 * tok_count + 2 * groups - 1) // (2 * groups))
    slot_count = groups * capacity
    target = pair_ids % groups
    matches = (target[:, None] == jnp.arange(groups, dtype=jnp.int32)[None, :]).astype(jnp.int32)
    before = jnp.sum((jnp.cumsum(matches, axis=0) - matches) * matches, axis=1)
    position = target * capacity + before
    placing = position[None, :] == jnp.arange(slot_count, dtype=jnp.int32)[:, None]
    placer = placing.astype(jnp.bfloat16)
    slot_pairs = jnp.sum(jnp.where(placing, pair_ids[None, :] + 1, 0), axis=1) - 1

    def route(values, extra):
        moved = jnp.dot(placer, values, preferred_element_type=jnp.float32).astype(jnp.bfloat16)
        rows = [moved.reshape(groups, capacity * piece // BLOCK, BLOCK)] + extra
        used = sum(r.shape[1] for r in rows)
        tile_rows = -(-used // 8) * 8
        if tile_rows > used:
            rows.append(jnp.zeros((groups, tile_rows - used, BLOCK), jnp.bfloat16))
        arrived = lax.all_to_all(
            jnp.concatenate(rows, axis=1), "dp", split_axis=0, concat_axis=0, tiled=True
        )
        return arrived, capacity * piece // BLOCK

    def widen(arrived, feat_rows):
        part = arrived[:, :feat_rows, :].reshape(slot_count, piece)
        gathered = lax.all_gather(part, "tensor", axis=0, tiled=False)
        shards = gathered.shape[0]
        return jnp.transpose(gathered, (1, 0, 2)).reshape(slot_count, shards * piece)

    pair_rows = jnp.broadcast_to(
        slot_pairs.astype(jnp.bfloat16).reshape(groups, capacity, 1), (groups, capacity, BLOCK)
    )
    arrived_tok, feat_rows = route(tokens, [pair_rows])
    pairs_here = arrived_tok[:, feat_rows:feat_rows + capacity, 0].reshape(slot_count).astype(jnp.int32)
    rows_in = widen(arrived_tok, feat_rows)
    arrived_cot, _ = route(cotangent, [])
    grad_rows = widen(arrived_cot, feat_rows)

    def send_back(values):
        returned = lax.all_to_all(
            values.reshape(groups, capacity * piece // BLOCK, BLOCK), "dp", split_axis=0, concat_axis=0, tiled=True
        )
        flattened = returned.reshape(slot_count, piece)
        return jnp.dot(placer.T, flattened, preferred_element_type=jnp.float32).astype(jnp.bfloat16)

    up_fwd, up_in = picked_masks(up_mask, pairs_here, (0, 2, 1))
    up_bwd, up_out = picked_masks(up_mask, pairs_here, (0, 1, 2))
    down_fwd, down_in = picked_masks(down_mask, pairs_here, (0, 2, 1))
    down_bwd, down_out = picked_masks(down_mask, pairs_here, (0, 1, 2))
    down_local = down_weight[0]

    before_act = masked_product(rows_in, up_fwd, up_in, up_weight, False, jnp.float32)
    activated, backward_function = jax.vjp(jax.nn.gelu, before_act)
    hidden = activated.astype(jnp.bfloat16)
    mixed_part = masked_product(hidden, down_fwd, down_in, down_local, False, jnp.bfloat16, piece)
    mixed_sum = settle(mixed_part)
    mixed = send_back(mixed_sum)
    grad_hidden = masked_product(grad_rows, down_bwd, down_out, down_local, True, jnp.float32)
    grad_pre = backward_function(grad_hidden)[0].astype(jnp.bfloat16)
    input_part = masked_product(grad_pre, up_bwd, up_out, up_weight, True, jnp.bfloat16, piece)
    input_sum = settle(input_part)

    return (mixed, send_back(input_sum))


def solution(mesh):
    return jax.shard_map(
        per_device,
        mesh=mesh,
        in_specs=(
            P("dp", "tensor"),
            P("dp", "tensor"),
            P("dp"),
            P(None, None, "tensor"),
            P(None, "tensor", None),
            P(None, "tensor"),
            P("dp", "tensor", None),
        ),
        out_specs=(P("dp", "tensor"), P("dp", "tensor")),
        check_vma=False,
    )
```

```python
import functools

import jax
import jax.numpy as jnp
from jax import lax
from jax.experimental import pallas as pl
from jax.sharding import PartitionSpec as P

BLOCK = 128
STEPS = 4


def picked_masks(mask_table, pairs_here, order):
    table = jnp.transpose(mask_table, order)
    pair_count, blocks_out, blocks_in = table.shape
    table = jnp.pad(table, ((0, 0), (0, 0), (0, BLOCK - blocks_in)))
    picker = (pairs_here[:, None] == jnp.arange(pair_count, dtype=jnp.int32)[None, :]).astype(
        jnp.bfloat16
    )
    flattened = table.reshape(pair_count, -1).astype(jnp.bfloat16)
    looked = jnp.dot(picker, flattened, preferred_element_type=jnp.float32).astype(jnp.bfloat16)
    looked = looked.reshape(pairs_here.shape[0], blocks_out, BLOCK)
    return jnp.transpose(looked, (1, 0, 2)), blocks_in


def masked_kernel(x_ref, m_ref, e_ref, w_ref, o_ref, *, per, turned, piece):
    x = x_ref[...]
    for b in range(per):
        spread = jnp.dot(m_ref[b], e_ref[...], preferred_element_type=jnp.float32).astype(x.dtype)
        masked = x * spread
        if turned:
            w = w_ref[b * BLOCK:(b + 1) * BLOCK, :]
            acc = lax.dot_general(
                masked, w, (((1,), (1,)), ((), ())), preferred_element_type=jnp.float32
            )
        else:
            w = w_ref[:, b * BLOCK:(b + 1) * BLOCK]
            acc = jnp.dot(masked, w, preferred_element_type=jnp.float32)
        if piece:
            at = b * BLOCK
            o_ref[at // piece, :, at % piece:at % piece + BLOCK] = acc.astype(o_ref.dtype)
        else:
            o_ref[:, b * BLOCK:(b + 1) * BLOCK] = acc.astype(o_ref.dtype)


def masked_product(x, masks, blocks_in, weight, turned, out_dtype, piece=0):
    rows, width = x.shape
    blocks_out = masks.shape[0]
    per = max(1, blocks_out // STEPS)
    steps = blocks_out // per
    cols = per * BLOCK
    blk = width // blocks_in
    expand = (
        jnp.arange(width, dtype=jnp.int32)[None, :] // blk == jnp.arange(BLOCK, dtype=jnp.int32)[:, None]
    ).astype(x.dtype)
    if turned:
        w_spec = pl.BlockSpec((cols, width), lambda j: (j, 0))
    else:
        w_spec = pl.BlockSpec((width, cols), lambda j: (0, j))
    if piece:
        out_spec = pl.BlockSpec((cols // piece, rows, piece), lambda j: (j, 0, 0))
        out_shape = (blocks_out * BLOCK // piece, rows, piece)
    else:
        out_spec = pl.BlockSpec((rows, cols), lambda j: (0, j))
        out_shape = (rows, blocks_out * BLOCK)
    return pl.pallas_call(
        functools.partial(masked_kernel, per=per, turned=turned, piece=piece),
        grid=(steps,),
        in_specs=[
            pl.BlockSpec((rows, width), lambda j: (0, 0)),
            pl.BlockSpec((per, rows, BLOCK), lambda j: (j, 0, 0)),
            pl.BlockSpec((BLOCK, width), lambda j: (0, 0)),
            w_spec,
        ],
        out_specs=out_spec,
        out_shape=jax.ShapeDtypeStruct(out_shape, out_dtype),
    )(x, masks, expand, weight)


def settle(part):
    arrived = lax.all_to_all(part, "tensor", split_axis=0, concat_axis=0, tiled=True)
    return jnp.sum(arrived.astype(jnp.float32), axis=0).astype(jnp.bfloat16)


def per_device(tokens, cotangent, pair_ids, up_mask, down_mask, up_weight, down_weight):
    groups = lax.axis_size("dp")
    tok_count, piece = tokens.shape
    capacity = max(2, (3 * tok_count + 2 * groups - 1) // (2 * groups))
    slot_count = groups * capacity
    target = pair_ids % groups
    matches = (target[:, None] == jnp.arange(groups, dtype=jnp.int32)[None, :]).astype(jnp.int32)
    before = jnp.sum((jnp.cumsum(matches, axis=0) - matches) * matches, axis=1)
    position = target * capacity + before
    placing = position[None, :] == jnp.arange(slot_count, dtype=jnp.int32)[:, None]
    placer = placing.astype(jnp.bfloat16)
    slot_pairs = jnp.sum(jnp.where(placing, pair_ids[None, :] + 1, 0), axis=1) - 1

    payload = jnp.concatenate([tokens, cotangent], axis=1)
    outgoing = jnp.dot(placer, payload, preferred_element_type=jnp.float32).astype(jnp.bfloat16)
    pair_cols = jnp.broadcast_to(slot_pairs.astype(jnp.bfloat16)[:, None], (slot_count, BLOCK))
    outgoing = jnp.concatenate([outgoing, pair_cols], axis=1)
    arrived = lax.all_to_all(
        outgoing.reshape(groups, capacity, -1), "dp", split_axis=0, concat_axis=0, tiled=True
    ).reshape(slot_count, -1)
    feats = arrived[:, :2 * piece]
    pairs_here = arrived[:, 2 * piece].astype(jnp.int32)

    both = jnp.stack([feats[:, :piece], feats[:, piece:]])
    gathered = lax.all_gather(both, "tensor", axis=0, tiled=False)
    shards = gathered.shape[0]
    gathered = jnp.transpose(gathered, (1, 2, 0, 3)).reshape(2, slot_count, shards * piece)
    rows_in, grad_rows = gathered[0], gathered[1]

    up_fwd, up_in = picked_masks(up_mask, pairs_here, (0, 2, 1))
    up_bwd, up_out = picked_masks(up_mask, pairs_here, (0, 1, 2))
    down_fwd, down_in = picked_masks(down_mask, pairs_here, (0, 2, 1))
    down_bwd, down_out = picked_masks(down_mask, pairs_here, (0, 1, 2))
    down_local = down_weight[0]

    before_act = masked_product(rows_in, up_fwd, up_in, up_weight, False, jnp.float32)
    activated, backward_function = jax.vjp(jax.nn.gelu, before_act)
    hidden = activated.astype(jnp.bfloat16)
    mixed_part = masked_product(hidden, down_fwd, down_in, down_local, False, jnp.bfloat16, piece)
    mixed_sum = settle(mixed_part)
    grad_hidden = masked_product(grad_rows, down_bwd, down_out, down_local, True, jnp.float32)
    grad_pre = backward_function(grad_hidden)[0].astype(jnp.bfloat16)
    input_part = masked_product(grad_pre, up_bwd, up_out, up_weight, True, jnp.bfloat16, piece)
    input_sum = settle(input_part)

    summed = jnp.stack([mixed_sum, input_sum])

    back = jnp.transpose(summed, (1, 0, 2)).reshape(groups, capacity * 2 * piece // BLOCK, BLOCK)
    returned = lax.all_to_all(back, "dp", split_axis=0, concat_axis=0, tiled=True)
    flattened = returned.reshape(slot_count, 2 * piece)
    results = jnp.dot(placer.T, flattened, preferred_element_type=jnp.float32).astype(jnp.bfloat16)
    return (results[:, :piece], results[:, piece:])


def solution(mesh):
    return jax.shard_map(
        per_device,
        mesh=mesh,
        in_specs=(
            P("dp", "tensor"),
            P("dp", "tensor"),
            P("dp"),
            P(None, None, "tensor"),
            P(None, "tensor", None),
            P(None, "tensor"),
            P("dp", "tensor", None),
        ),
        out_specs=(P("dp", "tensor"), P("dp", "tensor")),
        check_vma=False,
    )
```

```python
import functools

import jax
import jax.numpy as jnp
from jax import lax
from jax.experimental import pallas as pl
from jax.sharding import PartitionSpec as P

BLOCK = 128
STEPS = 4


def picked_masks(mask_table, pairs_here, order):
    table = jnp.transpose(mask_table, order)
    pair_count, blocks_out, blocks_in = table.shape
    table = jnp.pad(table, ((0, 0), (0, 0), (0, BLOCK - blocks_in)))
    picker = (pairs_here[:, None] == jnp.arange(pair_count, dtype=jnp.int32)[None, :]).astype(
        jnp.bfloat16
    )
    flattened = table.reshape(pair_count, -1).astype(jnp.bfloat16)
    looked = jnp.dot(picker, flattened, preferred_element_type=jnp.float32).astype(jnp.bfloat16)
    looked = looked.reshape(pairs_here.shape[0], blocks_out, BLOCK)
    return jnp.transpose(looked, (1, 0, 2)), blocks_in


def masked_kernel(x_ref, m_ref, e_ref, w_ref, o_ref, *, per, turned, piece):
    x = x_ref[...]
    for b in range(per):
        spread = jnp.dot(m_ref[b], e_ref[...], preferred_element_type=jnp.float32).astype(x.dtype)
        masked = x * spread
        if turned:
            w = w_ref[b * BLOCK:(b + 1) * BLOCK, :]
            acc = lax.dot_general(
                masked, w, (((1,), (1,)), ((), ())), preferred_element_type=jnp.float32
            )
        else:
            w = w_ref[:, b * BLOCK:(b + 1) * BLOCK]
            acc = jnp.dot(masked, w, preferred_element_type=jnp.float32)
        if piece:
            at = b * BLOCK
            o_ref[at // piece, :, at % piece:at % piece + BLOCK] = acc.astype(o_ref.dtype)
        else:
            o_ref[:, b * BLOCK:(b + 1) * BLOCK] = acc.astype(o_ref.dtype)


def masked_product(x, masks, blocks_in, weight, turned, out_dtype, piece=0):
    rows, width = x.shape
    blocks_out = masks.shape[0]
    per = max(1, blocks_out // STEPS)
    steps = blocks_out // per
    cols = per * BLOCK
    blk = width // blocks_in
    expand = (
        jnp.arange(width, dtype=jnp.int32)[None, :] // blk == jnp.arange(BLOCK, dtype=jnp.int32)[:, None]
    ).astype(x.dtype)
    if turned:
        w_spec = pl.BlockSpec((cols, width), lambda j: (j, 0))
    else:
        w_spec = pl.BlockSpec((width, cols), lambda j: (0, j))
    if piece:
        out_spec = pl.BlockSpec((cols // piece, rows, piece), lambda j: (j, 0, 0))
        out_shape = (blocks_out * BLOCK // piece, rows, piece)
    else:
        out_spec = pl.BlockSpec((rows, cols), lambda j: (0, j))
        out_shape = (rows, blocks_out * BLOCK)
    return pl.pallas_call(
        functools.partial(masked_kernel, per=per, turned=turned, piece=piece),
        grid=(steps,),
        in_specs=[
            pl.BlockSpec((rows, width), lambda j: (0, 0)),
            pl.BlockSpec((per, rows, BLOCK), lambda j: (j, 0, 0)),
            pl.BlockSpec((BLOCK, width), lambda j: (0, 0)),
            w_spec,
        ],
        out_specs=out_spec,
        out_shape=jax.ShapeDtypeStruct(out_shape, out_dtype),
    )(x, masks, expand, weight)


def settle(part):
    arrived = lax.all_to_all(part, "tensor", split_axis=0, concat_axis=0, tiled=True)
    return jnp.sum(arrived.astype(jnp.float32), axis=0).astype(jnp.bfloat16)


def per_device(tokens, cotangent, pair_ids, up_mask, down_mask, up_weight, down_weight):
    groups = lax.axis_size("dp")
    tok_count, piece = tokens.shape
    capacity = max(2, (3 * tok_count + 2 * groups - 1) // (2 * groups))
    slot_count = groups * capacity
    target = pair_ids % groups
    matches = (target[:, None] == jnp.arange(groups, dtype=jnp.int32)[None, :]).astype(jnp.int32)
    before = jnp.sum((jnp.cumsum(matches, axis=0) - matches) * matches, axis=1)
    position = target * capacity + before
    placing = position[None, :] == jnp.arange(slot_count, dtype=jnp.int32)[:, None]
    placer = placing.astype(jnp.bfloat16)
    slot_pairs = jnp.sum(jnp.where(placing, pair_ids[None, :] + 1, 0), axis=1) - 1

    payload = jnp.concatenate([tokens, cotangent], axis=1)
    outgoing = jnp.dot(placer, payload, preferred_element_type=jnp.float32).astype(jnp.bfloat16)
    pair_cols = jnp.broadcast_to(slot_pairs.astype(jnp.bfloat16)[:, None], (slot_count, BLOCK))
    outgoing = jnp.concatenate([outgoing, pair_cols], axis=1)
    arrived = lax.all_to_all(
        outgoing.reshape(groups, capacity, -1), "dp", split_axis=0, concat_axis=0, tiled=True
    ).reshape(slot_count, -1)
    feats = arrived[:, :2 * piece]
    pairs_here = arrived[:, 2 * piece].astype(jnp.int32)

    gathered = lax.all_gather(feats, "tensor", axis=0, tiled=False)
    shards = gathered.shape[0]
    gathered = gathered.reshape(shards, slot_count, 2, piece)
    gathered = jnp.transpose(gathered, (2, 1, 0, 3)).reshape(2, slot_count, shards * piece)
    rows_in, grad_rows = gathered[0], gathered[1]

    up_fwd, up_in = picked_masks(up_mask, pairs_here, (0, 2, 1))
    up_bwd, up_out = picked_masks(up_mask, pairs_here, (0, 1, 2))
    down_fwd, down_in = picked_masks(down_mask, pairs_here, (0, 2, 1))
    down_bwd, down_out = picked_masks(down_mask, pairs_here, (0, 1, 2))
    down_local = down_weight[0]

    before_act = masked_product(rows_in, up_fwd, up_in, up_weight, False, jnp.float32)
    activated, backward_function = jax.vjp(jax.nn.gelu, before_act)
    hidden = activated.astype(jnp.bfloat16)
    mixed_part = masked_product(hidden, down_fwd, down_in, down_local, False, jnp.bfloat16, piece)
    mixed_sum = settle(mixed_part)
    grad_hidden = masked_product(grad_rows, down_bwd, down_out, down_local, True, jnp.float32)
    grad_pre = backward_function(grad_hidden)[0].astype(jnp.bfloat16)
    input_part = masked_product(grad_pre, up_bwd, up_out, up_weight, True, jnp.bfloat16, piece)
    input_sum = settle(input_part)

    summed = jnp.stack([mixed_sum, input_sum])

    back = jnp.transpose(summed, (1, 0, 2)).reshape(groups, capacity * 2 * piece // BLOCK, BLOCK)
    returned = lax.all_to_all(back, "dp", split_axis=0, concat_axis=0, tiled=True)
    flattened = returned.reshape(slot_count, 2 * piece)
    results = jnp.dot(placer.T, flattened, preferred_element_type=jnp.float32).astype(jnp.bfloat16)
    return (results[:, :piece], results[:, piece:])


def solution(mesh):
    return jax.shard_map(
        per_device,
        mesh=mesh,
        in_specs=(
            P("dp", "tensor"),
            P("dp", "tensor"),
            P("dp"),
            P(None, None, "tensor"),
            P(None, "tensor", None),
            P(None, "tensor"),
            P("dp", "tensor", None),
        ),
        out_specs=(P("dp", "tensor"), P("dp", "tensor")),
        check_vma=False,
    )
```

```python
import functools

import jax
import jax.numpy as jnp
from jax import lax
from jax.experimental import pallas as pl
from jax.sharding import PartitionSpec as P

BLOCK = 128
STEPS = 4


def picked_masks(mask_table, pairs_here, order):
    table = jnp.transpose(mask_table, order)
    pair_count, blocks_out, blocks_in = table.shape
    table = jnp.pad(table, ((0, 0), (0, 0), (0, BLOCK - blocks_in)))
    picker = (pairs_here[:, None] == jnp.arange(pair_count, dtype=jnp.int32)[None, :]).astype(
        jnp.bfloat16
    )
    flattened = table.reshape(pair_count, -1).astype(jnp.bfloat16)
    looked = jnp.dot(picker, flattened, preferred_element_type=jnp.float32).astype(jnp.bfloat16)
    looked = looked.reshape(pairs_here.shape[0], blocks_out, BLOCK)
    return jnp.transpose(looked, (1, 0, 2)), blocks_in


def masked_kernel(x_ref, m_ref, w_ref, o_ref, *, per, turned, piece, blocks_in):
    accs = [None] * per
    for i in range(blocks_in):
        xi = x_ref[:, i * BLOCK:(i + 1) * BLOCK]
        if not turned:
            y = jnp.dot(xi, w_ref[i * BLOCK:(i + 1) * BLOCK, :], preferred_element_type=jnp.float32)
        for b in range(per):
            if turned:
                w = w_ref[b * BLOCK:(b + 1) * BLOCK, i * BLOCK:(i + 1) * BLOCK]
                yb = lax.dot_general(xi, w, (((1,), (1,)), ((), ())), preferred_element_type=jnp.float32)
            else:
                yb = y[:, b * BLOCK:(b + 1) * BLOCK]
            term = yb * m_ref[b, :, i:i + 1]
            accs[b] = term if accs[b] is None else accs[b] + term
    for b in range(per):
        if piece:
            at = b * BLOCK
            o_ref[at // piece, :, at % piece:at % piece + BLOCK] = accs[b].astype(o_ref.dtype)
        else:
            o_ref[:, b * BLOCK:(b + 1) * BLOCK] = accs[b].astype(o_ref.dtype)


def masked_product(x, masks, blocks_in, weight, turned, out_dtype, piece=0):
    rows, width = x.shape
    blocks_out = masks.shape[0]
    per = max(1, blocks_out // STEPS)
    steps = blocks_out // per
    cols = per * BLOCK
    masks = masks.astype(jnp.float32)
    if turned:
        w_spec = pl.BlockSpec((cols, width), lambda j: (j, 0))
    else:
        w_spec = pl.BlockSpec((width, cols), lambda j: (0, j))
    if piece:
        out_spec = pl.BlockSpec((cols // piece, rows, piece), lambda j: (j, 0, 0))
        out_shape = (blocks_out * BLOCK // piece, rows, piece)
    else:
        out_spec = pl.BlockSpec((rows, cols), lambda j: (0, j))
        out_shape = (rows, blocks_out * BLOCK)
    return pl.pallas_call(
        functools.partial(masked_kernel, per=per, turned=turned, piece=piece, blocks_in=blocks_in),
        grid=(steps,),
        in_specs=[
            pl.BlockSpec((rows, width), lambda j: (0, 0)),
            pl.BlockSpec((per, rows, BLOCK), lambda j: (j, 0, 0)),
            w_spec,
        ],
        out_specs=out_spec,
        out_shape=jax.ShapeDtypeStruct(out_shape, out_dtype),
    )(x, masks, weight)


def settle(part):
    arrived = lax.all_to_all(part, "tensor", split_axis=0, concat_axis=0, tiled=True)
    return jnp.sum(arrived.astype(jnp.float32), axis=0).astype(jnp.bfloat16)


def per_device(tokens, cotangent, pair_ids, up_mask, down_mask, up_weight, down_weight):
    groups = lax.axis_size("dp")
    tok_count, piece = tokens.shape
    capacity = max(2, (3 * tok_count + 2 * groups - 1) // (2 * groups))
    slot_count = groups * capacity
    target = pair_ids % groups
    matches = (target[:, None] == jnp.arange(groups, dtype=jnp.int32)[None, :]).astype(jnp.int32)
    before = jnp.sum((jnp.cumsum(matches, axis=0) - matches) * matches, axis=1)
    position = target * capacity + before
    placing = position[None, :] == jnp.arange(slot_count, dtype=jnp.int32)[:, None]
    placer = placing.astype(jnp.bfloat16)
    slot_pairs = jnp.sum(jnp.where(placing, pair_ids[None, :] + 1, 0), axis=1) - 1

    payload = jnp.concatenate([tokens, cotangent], axis=1)
    outgoing = jnp.dot(placer, payload, preferred_element_type=jnp.float32).astype(jnp.bfloat16)
    pair_cols = jnp.broadcast_to(slot_pairs.astype(jnp.bfloat16)[:, None], (slot_count, BLOCK))
    outgoing = jnp.concatenate([outgoing, pair_cols], axis=1)
    arrived = lax.all_to_all(
        outgoing.reshape(groups, capacity, -1), "dp", split_axis=0, concat_axis=0, tiled=True
    ).reshape(slot_count, -1)
    feats = arrived[:, :2 * piece]
    pairs_here = arrived[:, 2 * piece].astype(jnp.int32)

    both = jnp.stack([feats[:, :piece], feats[:, piece:]])
    gathered = lax.all_gather(both, "tensor", axis=0, tiled=False)
    shards = gathered.shape[0]
    gathered = jnp.transpose(gathered, (1, 2, 0, 3)).reshape(2, slot_count, shards * piece)
    rows_in, grad_rows = gathered[0], gathered[1]

    up_fwd, up_in = picked_masks(up_mask, pairs_here, (0, 2, 1))
    up_bwd, up_out = picked_masks(up_mask, pairs_here, (0, 1, 2))
    down_fwd, down_in = picked_masks(down_mask, pairs_here, (0, 2, 1))
    down_bwd, down_out = picked_masks(down_mask, pairs_here, (0, 1, 2))
    down_local = down_weight[0]

    before_act = masked_product(rows_in, up_fwd, up_in, up_weight, False, jnp.float32)
    activated, backward_function = jax.vjp(jax.nn.gelu, before_act)
    hidden = activated.astype(jnp.bfloat16)
    mixed_part = masked_product(hidden, down_fwd, down_in, down_local, False, jnp.bfloat16, piece)
    mixed_sum = settle(mixed_part)
    grad_hidden = masked_product(grad_rows, down_bwd, down_out, down_local, True, jnp.float32)
    grad_pre = backward_function(grad_hidden)[0].astype(jnp.bfloat16)
    input_part = masked_product(grad_pre, up_bwd, up_out, up_weight, True, jnp.bfloat16, piece)
    input_sum = settle(input_part)

    summed = jnp.stack([mixed_sum, input_sum])

    back = jnp.transpose(summed, (1, 0, 2)).reshape(groups, capacity * 2 * piece // BLOCK, BLOCK)
    returned = lax.all_to_all(back, "dp", split_axis=0, concat_axis=0, tiled=True)
    flattened = returned.reshape(slot_count, 2 * piece)
    results = jnp.dot(placer.T, flattened, preferred_element_type=jnp.float32).astype(jnp.bfloat16)
    return (results[:, :piece], results[:, piece:])


def solution(mesh):
    return jax.shard_map(
        per_device,
        mesh=mesh,
        in_specs=(
            P("dp", "tensor"),
            P("dp", "tensor"),
            P("dp"),
            P(None, None, "tensor"),
            P(None, "tensor", None),
            P(None, "tensor"),
            P("dp", "tensor", None),
        ),
        out_specs=(P("dp", "tensor"), P("dp", "tensor")),
        check_vma=False,
    )
```

```python
import functools

import jax
import jax.numpy as jnp
from jax import lax
from jax.experimental import pallas as pl
from jax.sharding import PartitionSpec as P

BLOCK = 128
STEPS = 4


def picked_masks(mask_table, pairs_here, order):
    table = jnp.transpose(mask_table, order)
    pair_count, blocks_out, blocks_in = table.shape
    table = jnp.pad(table, ((0, 0), (0, 0), (0, BLOCK - blocks_in)))
    picker = (pairs_here[:, None] == jnp.arange(pair_count, dtype=jnp.int32)[None, :]).astype(
        jnp.bfloat16
    )
    flattened = table.reshape(pair_count, -1).astype(jnp.bfloat16)
    looked = jnp.dot(picker, flattened, preferred_element_type=jnp.float32).astype(jnp.bfloat16)
    looked = looked.reshape(pairs_here.shape[0], blocks_out, BLOCK)
    return jnp.transpose(looked, (1, 0, 2)), blocks_in


def masked_kernel(x_ref, m_ref, w_ref, o_ref, *act_ref, per, turned, piece, blocks_in):
    accs = [None] * per
    for i in range(blocks_in):
        xi = x_ref[:, i * BLOCK:(i + 1) * BLOCK]
        if not turned:
            y = jnp.dot(xi, w_ref[i * BLOCK:(i + 1) * BLOCK, :], preferred_element_type=jnp.float32)
        for b in range(per):
            if turned:
                w = w_ref[b * BLOCK:(b + 1) * BLOCK, i * BLOCK:(i + 1) * BLOCK]
                yb = lax.dot_general(xi, w, (((1,), (1,)), ((), ())), preferred_element_type=jnp.float32)
            else:
                yb = y[:, b * BLOCK:(b + 1) * BLOCK]
            term = yb * m_ref[b, :, i:i + 1]
            accs[b] = term if accs[b] is None else accs[b] + term
    for b in range(per):
        if piece:
            at = b * BLOCK
            o_ref[at // piece, :, at % piece:at % piece + BLOCK] = accs[b].astype(o_ref.dtype)
        else:
            o_ref[:, b * BLOCK:(b + 1) * BLOCK] = accs[b].astype(o_ref.dtype)
        if act_ref:
            act_ref[0][:, b * BLOCK:(b + 1) * BLOCK] = jax.nn.gelu(accs[b]).astype(act_ref[0].dtype)


def masked_product(x, masks, blocks_in, weight, turned, out_dtype, piece=0, act=False):
    rows, width = x.shape
    blocks_out = masks.shape[0]
    per = max(1, blocks_out // STEPS)
    steps = blocks_out // per
    cols = per * BLOCK
    masks = masks.astype(jnp.float32)
    if turned:
        w_spec = pl.BlockSpec((cols, width), lambda j: (j, 0))
    else:
        w_spec = pl.BlockSpec((width, cols), lambda j: (0, j))
    if piece:
        out_spec = pl.BlockSpec((cols // piece, rows, piece), lambda j: (j, 0, 0))
        out_shape = (blocks_out * BLOCK // piece, rows, piece)
    else:
        out_spec = pl.BlockSpec((rows, cols), lambda j: (0, j))
        out_shape = (rows, blocks_out * BLOCK)
    return pl.pallas_call(
        functools.partial(masked_kernel, per=per, turned=turned, piece=piece, blocks_in=blocks_in),
        grid=(steps,),
        in_specs=[
            pl.BlockSpec((rows, width), lambda j: (0, 0)),
            pl.BlockSpec((per, rows, BLOCK), lambda j: (j, 0, 0)),
            w_spec,
        ],
        out_specs=[out_spec, out_spec] if act else out_spec,
        out_shape=(
            [jax.ShapeDtypeStruct(out_shape, out_dtype), jax.ShapeDtypeStruct(out_shape, x.dtype)]
            if act
            else jax.ShapeDtypeStruct(out_shape, out_dtype)
        ),
    )(x, masks, weight)


def settle(part):
    arrived = lax.all_to_all(part, "tensor", split_axis=0, concat_axis=0, tiled=True)
    return jnp.sum(arrived.astype(jnp.float32), axis=0).astype(jnp.bfloat16)


def per_device(tokens, cotangent, pair_ids, up_mask, down_mask, up_weight, down_weight):
    groups = lax.axis_size("dp")
    tok_count, piece = tokens.shape
    capacity = max(2, (3 * tok_count + 2 * groups - 1) // (2 * groups))
    slot_count = groups * capacity
    target = pair_ids % groups
    matches = (target[:, None] == jnp.arange(groups, dtype=jnp.int32)[None, :]).astype(jnp.int32)
    before = jnp.sum((jnp.cumsum(matches, axis=0) - matches) * matches, axis=1)
    position = target * capacity + before
    placing = position[None, :] == jnp.arange(slot_count, dtype=jnp.int32)[:, None]
    placer = placing.astype(jnp.bfloat16)
    slot_pairs = jnp.sum(jnp.where(placing, pair_ids[None, :] + 1, 0), axis=1) - 1

    payload = jnp.concatenate([tokens, cotangent], axis=1)
    outgoing = jnp.dot(placer, payload, preferred_element_type=jnp.float32).astype(jnp.bfloat16)
    pair_cols = jnp.broadcast_to(slot_pairs.astype(jnp.bfloat16)[:, None], (slot_count, BLOCK))
    outgoing = jnp.concatenate([outgoing, pair_cols], axis=1)
    arrived = lax.all_to_all(
        outgoing.reshape(groups, capacity, -1), "dp", split_axis=0, concat_axis=0, tiled=True
    ).reshape(slot_count, -1)
    feats = arrived[:, :2 * piece]
    pairs_here = arrived[:, 2 * piece].astype(jnp.int32)

    both = jnp.stack([feats[:, :piece], feats[:, piece:]])
    gathered = lax.all_gather(both, "tensor", axis=0, tiled=False)
    shards = gathered.shape[0]
    gathered = jnp.transpose(gathered, (1, 2, 0, 3)).reshape(2, slot_count, shards * piece)
    rows_in, grad_rows = gathered[0], gathered[1]

    up_fwd, up_in = picked_masks(up_mask, pairs_here, (0, 2, 1))
    up_bwd, up_out = picked_masks(up_mask, pairs_here, (0, 1, 2))
    down_fwd, down_in = picked_masks(down_mask, pairs_here, (0, 2, 1))
    down_bwd, down_out = picked_masks(down_mask, pairs_here, (0, 1, 2))
    down_local = down_weight[0]

    before_act, hidden = masked_product(rows_in, up_fwd, up_in, up_weight, False, jnp.float32, act=True)
    _, backward_function = jax.vjp(jax.nn.gelu, before_act)
    mixed_part = masked_product(hidden, down_fwd, down_in, down_local, False, jnp.bfloat16, piece)
    mixed_sum = settle(mixed_part)
    grad_hidden = masked_product(grad_rows, down_bwd, down_out, down_local, True, jnp.float32)
    grad_pre = backward_function(grad_hidden)[0].astype(jnp.bfloat16)
    input_part = masked_product(grad_pre, up_bwd, up_out, up_weight, True, jnp.bfloat16, piece)
    input_sum = settle(input_part)

    summed = jnp.stack([mixed_sum, input_sum])

    back = jnp.transpose(summed, (1, 0, 2)).reshape(groups, capacity * 2 * piece // BLOCK, BLOCK)
    returned = lax.all_to_all(back, "dp", split_axis=0, concat_axis=0, tiled=True)
    flattened = returned.reshape(slot_count, 2 * piece)
    results = jnp.dot(placer.T, flattened, preferred_element_type=jnp.float32).astype(jnp.bfloat16)
    return (results[:, :piece], results[:, piece:])


def solution(mesh):
    return jax.shard_map(
        per_device,
        mesh=mesh,
        in_specs=(
            P("dp", "tensor"),
            P("dp", "tensor"),
            P("dp"),
            P(None, None, "tensor"),
            P(None, "tensor", None),
            P(None, "tensor"),
            P("dp", "tensor", None),
        ),
        out_specs=(P("dp", "tensor"), P("dp", "tensor")),
        check_vma=False,
    )
```

```python
import functools

import jax
import jax.numpy as jnp
from jax import lax
from jax.experimental import pallas as pl
from jax.sharding import PartitionSpec as P

BLOCK = 128
STEPS = 4


def picked_masks(mask_table, pairs_here, order):
    table = jnp.transpose(mask_table, order)
    pair_count, blocks_out, blocks_in = table.shape
    table = jnp.pad(table, ((0, 0), (0, 0), (0, BLOCK - blocks_in)))
    picker = (pairs_here[:, None] == jnp.arange(pair_count, dtype=jnp.int32)[None, :]).astype(
        jnp.bfloat16
    )
    flattened = table.reshape(pair_count, -1).astype(jnp.bfloat16)
    looked = jnp.dot(picker, flattened, preferred_element_type=jnp.float32).astype(jnp.bfloat16)
    looked = looked.reshape(pairs_here.shape[0], blocks_out, BLOCK)
    return jnp.transpose(looked, (1, 0, 2)), blocks_in


def masked_kernel(x_ref, m_ref, w_ref, *refs, per, turned, piece, blocks_in, act, grad):
    pre_ref = refs[0] if grad else None
    o_ref = refs[1] if grad else refs[0]
    act_ref = refs[-1:] if act else ()
    accs = [None] * per
    for i in range(blocks_in):
        xi = x_ref[:, i * BLOCK:(i + 1) * BLOCK]
        if not turned:
            y = jnp.dot(xi, w_ref[i * BLOCK:(i + 1) * BLOCK, :], preferred_element_type=jnp.float32)
        for b in range(per):
            if turned:
                w = w_ref[b * BLOCK:(b + 1) * BLOCK, i * BLOCK:(i + 1) * BLOCK]
                yb = lax.dot_general(xi, w, (((1,), (1,)), ((), ())), preferred_element_type=jnp.float32)
            else:
                yb = y[:, b * BLOCK:(b + 1) * BLOCK]
            term = yb * m_ref[b, :, i:i + 1]
            accs[b] = term if accs[b] is None else accs[b] + term
    for b in range(per):
        if piece:
            at = b * BLOCK
            o_ref[at // piece, :, at % piece:at % piece + BLOCK] = accs[b].astype(o_ref.dtype)
        elif grad:
            _, backward_function = jax.vjp(jax.nn.gelu, pre_ref[:, b * BLOCK:(b + 1) * BLOCK])
            o_ref[:, b * BLOCK:(b + 1) * BLOCK] = backward_function(accs[b])[0].astype(o_ref.dtype)
        else:
            o_ref[:, b * BLOCK:(b + 1) * BLOCK] = accs[b].astype(o_ref.dtype)
        if act_ref:
            act_ref[0][:, b * BLOCK:(b + 1) * BLOCK] = jax.nn.gelu(accs[b]).astype(act_ref[0].dtype)


def masked_product(x, masks, blocks_in, weight, turned, out_dtype, piece=0, act=False, grad_of=None):
    rows, width = x.shape
    blocks_out = masks.shape[0]
    per = max(1, blocks_out // STEPS)
    steps = blocks_out // per
    cols = per * BLOCK
    masks = masks.astype(jnp.float32)
    if turned:
        w_spec = pl.BlockSpec((cols, width), lambda j: (j, 0))
    else:
        w_spec = pl.BlockSpec((width, cols), lambda j: (0, j))
    if piece:
        out_spec = pl.BlockSpec((cols // piece, rows, piece), lambda j: (j, 0, 0))
        out_shape = (blocks_out * BLOCK // piece, rows, piece)
    else:
        out_spec = pl.BlockSpec((rows, cols), lambda j: (0, j))
        out_shape = (rows, blocks_out * BLOCK)
    grad = grad_of is not None
    extra = [grad_of] if grad else []
    return pl.pallas_call(
        functools.partial(
            masked_kernel, per=per, turned=turned, piece=piece, blocks_in=blocks_in, act=act, grad=grad
        ),
        grid=(steps,),
        in_specs=[
            pl.BlockSpec((rows, width), lambda j: (0, 0)),
            pl.BlockSpec((per, rows, BLOCK), lambda j: (j, 0, 0)),
            w_spec,
        ] + [out_spec] * len(extra),
        out_specs=[out_spec, out_spec] if act else out_spec,
        out_shape=(
            [jax.ShapeDtypeStruct(out_shape, out_dtype), jax.ShapeDtypeStruct(out_shape, x.dtype)]
            if act
            else jax.ShapeDtypeStruct(out_shape, out_dtype)
        ),
    )(x, masks, weight, *extra)


def settle(part):
    arrived = lax.all_to_all(part, "tensor", split_axis=0, concat_axis=0, tiled=True)
    return jnp.sum(arrived.astype(jnp.float32), axis=0).astype(jnp.bfloat16)


def per_device(tokens, cotangent, pair_ids, up_mask, down_mask, up_weight, down_weight):
    groups = lax.axis_size("dp")
    tok_count, piece = tokens.shape
    capacity = max(2, (3 * tok_count + 2 * groups - 1) // (2 * groups))
    slot_count = groups * capacity
    target = pair_ids % groups
    matches = (target[:, None] == jnp.arange(groups, dtype=jnp.int32)[None, :]).astype(jnp.int32)
    before = jnp.sum((jnp.cumsum(matches, axis=0) - matches) * matches, axis=1)
    position = target * capacity + before
    placing = position[None, :] == jnp.arange(slot_count, dtype=jnp.int32)[:, None]
    placer = placing.astype(jnp.bfloat16)
    slot_pairs = jnp.sum(jnp.where(placing, pair_ids[None, :] + 1, 0), axis=1) - 1

    payload = jnp.concatenate([tokens, cotangent], axis=1)
    outgoing = jnp.dot(placer, payload, preferred_element_type=jnp.float32).astype(jnp.bfloat16)
    pair_cols = jnp.broadcast_to(slot_pairs.astype(jnp.bfloat16)[:, None], (slot_count, BLOCK))
    outgoing = jnp.concatenate([outgoing, pair_cols], axis=1)
    arrived = lax.all_to_all(
        outgoing.reshape(groups, capacity, -1), "dp", split_axis=0, concat_axis=0, tiled=True
    ).reshape(slot_count, -1)
    feats = arrived[:, :2 * piece]
    pairs_here = arrived[:, 2 * piece].astype(jnp.int32)

    both = jnp.stack([feats[:, :piece], feats[:, piece:]])
    gathered = lax.all_gather(both, "tensor", axis=0, tiled=False)
    shards = gathered.shape[0]
    gathered = jnp.transpose(gathered, (1, 2, 0, 3)).reshape(2, slot_count, shards * piece)
    rows_in, grad_rows = gathered[0], gathered[1]

    up_fwd, up_in = picked_masks(up_mask, pairs_here, (0, 2, 1))
    up_bwd, up_out = picked_masks(up_mask, pairs_here, (0, 1, 2))
    down_fwd, down_in = picked_masks(down_mask, pairs_here, (0, 2, 1))
    down_bwd, down_out = picked_masks(down_mask, pairs_here, (0, 1, 2))
    down_local = down_weight[0]

    before_act, hidden = masked_product(rows_in, up_fwd, up_in, up_weight, False, jnp.float32, act=True)
    mixed_part = masked_product(hidden, down_fwd, down_in, down_local, False, jnp.bfloat16, piece)
    mixed_sum = settle(mixed_part)
    grad_pre = masked_product(
        grad_rows, down_bwd, down_out, down_local, True, jnp.bfloat16, grad_of=before_act
    )
    input_part = masked_product(grad_pre, up_bwd, up_out, up_weight, True, jnp.bfloat16, piece)
    input_sum = settle(input_part)

    summed = jnp.stack([mixed_sum, input_sum])

    back = jnp.transpose(summed, (1, 0, 2)).reshape(groups, capacity * 2 * piece // BLOCK, BLOCK)
    returned = lax.all_to_all(back, "dp", split_axis=0, concat_axis=0, tiled=True)
    flattened = returned.reshape(slot_count, 2 * piece)
    results = jnp.dot(placer.T, flattened, preferred_element_type=jnp.float32).astype(jnp.bfloat16)
    return (results[:, :piece], results[:, piece:])


def solution(mesh):
    return jax.shard_map(
        per_device,
        mesh=mesh,
        in_specs=(
            P("dp", "tensor"),
            P("dp", "tensor"),
            P("dp"),
            P(None, None, "tensor"),
            P(None, "tensor", None),
            P(None, "tensor"),
            P("dp", "tensor", None),
        ),
        out_specs=(P("dp", "tensor"), P("dp", "tensor")),
        check_vma=False,
    )
```

```python
import functools

import jax
import jax.numpy as jnp
from jax import lax
from jax.experimental import pallas as pl
from jax.sharding import PartitionSpec as P

BLOCK = 128
STEPS = 2


def picked_masks(mask_table, pairs_here, order):
    table = jnp.transpose(mask_table, order)
    pair_count, blocks_out, blocks_in = table.shape
    table = jnp.pad(table, ((0, 0), (0, 0), (0, BLOCK - blocks_in)))
    picker = (pairs_here[:, None] == jnp.arange(pair_count, dtype=jnp.int32)[None, :]).astype(
        jnp.bfloat16
    )
    flattened = table.reshape(pair_count, -1).astype(jnp.bfloat16)
    looked = jnp.dot(picker, flattened, preferred_element_type=jnp.float32).astype(jnp.bfloat16)
    looked = looked.reshape(pairs_here.shape[0], blocks_out, BLOCK)
    return jnp.transpose(looked, (1, 0, 2)), blocks_in


def masked_kernel(x_ref, m_ref, w_ref, *refs, per, turned, piece, blocks_in, act, grad):
    pre_ref = refs[0] if grad else None
    o_ref = refs[1] if grad else refs[0]
    act_ref = refs[-1:] if act else ()
    accs = [None] * per
    for i in range(blocks_in):
        xi = x_ref[:, i * BLOCK:(i + 1) * BLOCK]
        if not turned:
            y = jnp.dot(xi, w_ref[i * BLOCK:(i + 1) * BLOCK, :], preferred_element_type=jnp.float32)
        for b in range(per):
            if turned:
                w = w_ref[b * BLOCK:(b + 1) * BLOCK, i * BLOCK:(i + 1) * BLOCK]
                yb = lax.dot_general(xi, w, (((1,), (1,)), ((), ())), preferred_element_type=jnp.float32)
            else:
                yb = y[:, b * BLOCK:(b + 1) * BLOCK]
            term = yb * m_ref[b, :, i:i + 1]
            accs[b] = term if accs[b] is None else accs[b] + term
    for b in range(per):
        if piece:
            at = b * BLOCK
            o_ref[at // piece, :, at % piece:at % piece + BLOCK] = accs[b].astype(o_ref.dtype)
        elif grad:
            _, backward_function = jax.vjp(jax.nn.gelu, pre_ref[:, b * BLOCK:(b + 1) * BLOCK])
            o_ref[:, b * BLOCK:(b + 1) * BLOCK] = backward_function(accs[b])[0].astype(o_ref.dtype)
        else:
            o_ref[:, b * BLOCK:(b + 1) * BLOCK] = accs[b].astype(o_ref.dtype)
        if act_ref:
            act_ref[0][:, b * BLOCK:(b + 1) * BLOCK] = jax.nn.gelu(accs[b]).astype(act_ref[0].dtype)


def masked_product(x, masks, blocks_in, weight, turned, out_dtype, piece=0, act=False, grad_of=None):
    rows, width = x.shape
    blocks_out = masks.shape[0]
    per = max(1, blocks_out // STEPS)
    steps = blocks_out // per
    cols = per * BLOCK
    masks = masks.astype(jnp.float32)
    if turned:
        w_spec = pl.BlockSpec((cols, width), lambda j: (j, 0))
    else:
        w_spec = pl.BlockSpec((width, cols), lambda j: (0, j))
    if piece:
        out_spec = pl.BlockSpec((cols // piece, rows, piece), lambda j: (j, 0, 0))
        out_shape = (blocks_out * BLOCK // piece, rows, piece)
    else:
        out_spec = pl.BlockSpec((rows, cols), lambda j: (0, j))
        out_shape = (rows, blocks_out * BLOCK)
    grad = grad_of is not None
    extra = [grad_of] if grad else []
    return pl.pallas_call(
        functools.partial(
            masked_kernel, per=per, turned=turned, piece=piece, blocks_in=blocks_in, act=act, grad=grad
        ),
        grid=(steps,),
        in_specs=[
            pl.BlockSpec((rows, width), lambda j: (0, 0)),
            pl.BlockSpec((per, rows, BLOCK), lambda j: (j, 0, 0)),
            w_spec,
        ] + [out_spec] * len(extra),
        out_specs=[out_spec, out_spec] if act else out_spec,
        out_shape=(
            [jax.ShapeDtypeStruct(out_shape, out_dtype), jax.ShapeDtypeStruct(out_shape, x.dtype)]
            if act
            else jax.ShapeDtypeStruct(out_shape, out_dtype)
        ),
    )(x, masks, weight, *extra)


def settle(part):
    arrived = lax.all_to_all(part, "tensor", split_axis=0, concat_axis=0, tiled=True)
    return jnp.sum(arrived.astype(jnp.float32), axis=0).astype(jnp.bfloat16)


def per_device(tokens, cotangent, pair_ids, up_mask, down_mask, up_weight, down_weight):
    groups = lax.axis_size("dp")
    tok_count, piece = tokens.shape
    capacity = max(2, (3 * tok_count + 2 * groups - 1) // (2 * groups))
    slot_count = groups * capacity
    target = pair_ids % groups
    matches = (target[:, None] == jnp.arange(groups, dtype=jnp.int32)[None, :]).astype(jnp.int32)
    before = jnp.sum((jnp.cumsum(matches, axis=0) - matches) * matches, axis=1)
    position = target * capacity + before
    placing = position[None, :] == jnp.arange(slot_count, dtype=jnp.int32)[:, None]
    placer = placing.astype(jnp.bfloat16)
    slot_pairs = jnp.sum(jnp.where(placing, pair_ids[None, :] + 1, 0), axis=1) - 1

    payload = jnp.concatenate([tokens, cotangent], axis=1)
    outgoing = jnp.dot(placer, payload, preferred_element_type=jnp.float32).astype(jnp.bfloat16)
    pair_cols = jnp.broadcast_to(slot_pairs.astype(jnp.bfloat16)[:, None], (slot_count, BLOCK))
    outgoing = jnp.concatenate([outgoing, pair_cols], axis=1)
    arrived = lax.all_to_all(
        outgoing.reshape(groups, capacity, -1), "dp", split_axis=0, concat_axis=0, tiled=True
    ).reshape(slot_count, -1)
    feats = arrived[:, :2 * piece]
    pairs_here = arrived[:, 2 * piece].astype(jnp.int32)

    both = jnp.stack([feats[:, :piece], feats[:, piece:]])
    gathered = lax.all_gather(both, "tensor", axis=0, tiled=False)
    shards = gathered.shape[0]
    gathered = jnp.transpose(gathered, (1, 2, 0, 3)).reshape(2, slot_count, shards * piece)
    rows_in, grad_rows = gathered[0], gathered[1]

    up_fwd, up_in = picked_masks(up_mask, pairs_here, (0, 2, 1))
    up_bwd, up_out = picked_masks(up_mask, pairs_here, (0, 1, 2))
    down_fwd, down_in = picked_masks(down_mask, pairs_here, (0, 2, 1))
    down_bwd, down_out = picked_masks(down_mask, pairs_here, (0, 1, 2))
    down_local = down_weight[0]

    before_act, hidden = masked_product(rows_in, up_fwd, up_in, up_weight, False, jnp.float32, act=True)
    mixed_part = masked_product(hidden, down_fwd, down_in, down_local, False, jnp.bfloat16, piece)
    mixed_sum = settle(mixed_part)
    grad_pre = masked_product(
        grad_rows, down_bwd, down_out, down_local, True, jnp.bfloat16, grad_of=before_act
    )
    input_part = masked_product(grad_pre, up_bwd, up_out, up_weight, True, jnp.bfloat16, piece)
    input_sum = settle(input_part)

    summed = jnp.stack([mixed_sum, input_sum])

    back = jnp.transpose(summed, (1, 0, 2)).reshape(groups, capacity * 2 * piece // BLOCK, BLOCK)
    returned = lax.all_to_all(back, "dp", split_axis=0, concat_axis=0, tiled=True)
    flattened = returned.reshape(slot_count, 2 * piece)
    results = jnp.dot(placer.T, flattened, preferred_element_type=jnp.float32).astype(jnp.bfloat16)
    return (results[:, :piece], results[:, piece:])


def solution(mesh):
    return jax.shard_map(
        per_device,
        mesh=mesh,
        in_specs=(
            P("dp", "tensor"),
            P("dp", "tensor"),
            P("dp"),
            P(None, None, "tensor"),
            P(None, "tensor", None),
            P(None, "tensor"),
            P("dp", "tensor", None),
        ),
        out_specs=(P("dp", "tensor"), P("dp", "tensor")),
        check_vma=False,
    )
```
